512 devices in a mesh: pb: 32 (over x, y), kv: 16 (over z, core).
Axes of the slice: x: 4, y: 8, z: 8, core: 2. Of those that a mesh axis runs over, the one named last changes fastest.
Arguments:
- queries: bfloat16 [2, 8192, 128], P(None, 'pb'), may hold values from -600 to 600
- cache_keys: bfloat16 [2, 16384, 128], P(None, 'kv'), may hold values from -6 to 6
- cache_values: bfloat16 [2, 16384, 128], P(None, 'kv'), may hold values from -6 to 6
- selected: int32 [2, 2048], replicated, may hold values from 0 to 16383, as said below
Outputs:
- new_values: float32 [2, 2048, 128], P(None, 'kv')
- fit_residual: float32 [2, 2048, 128], P(None, 'kv')
The draws below stay inside these ranges and needn't reach their ends.
Inputs may be any that keep to these rules, and one draw needn't show every extreme that they name: `selected`: each head's row holds 2048 different key positions; the cache's shards hold unequal numbers of them.
All inputs are finite; a program needn't handle non-finite values.
Results may differ from the reference program's by a relative error of at most 0.0049.
Values may be sent and summed in bfloat16 or wider, within the bound.
No kernel may reach another device: no remote copies, remote signals or barrier semaphores. Data moves between devices by JAX's collectives and lax.ppermute only.
A program may use at most 64 MiB of HBM per device.

```python
import math
import jax
import jax.numpy as jnp
from jax import lax

HEADS = 2
D = 128
M = 2048
STEPS = 3
KEY_DEV = 1024
NQ = 8192
NK = 16384


def draw_queries(key, part):
    rows = jnp.arange(NQ, dtype=jnp.int32)
    offset = jax.random.randint(jax.random.fold_in(key, 5), (HEADS, 1), 0, 32)
    picks = (rows[None, :] % 32 == offset)[:, :, None]
    base = jnp.clip(2.0 * jax.random.normal(key, (HEADS, NQ, D), jnp.float32), -12.0, 12.0)
    boost = jax.random.uniform(jax.random.fold_in(key, 11), (HEADS, NQ, 1), jnp.float32, 25.0, 50.0)
    base = base * jnp.where(picks, boost, 1.0)
    return base.astype(jnp.bfloat16)


def draw_selected(key, part):
    shard_count = NK // KEY_DEV
    bias = jax.random.randint(jax.random.fold_in(key, 1), (HEADS, shard_count), 0, 4)
    noise = jax.random.randint(jax.random.fold_in(key, 2), (HEADS, NK), 0, 1024)
    positions = jnp.arange(NK, dtype=jnp.int32)
    owner = positions // KEY_DEV
    priority = (noise + 400 * bias[:, owner]) * NK + positions[None, :]
    _, picked = lax.top_k(priority, M)
    return picked.astype(jnp.int32)


def block_levels(stream_key, extent, split, least, top_value):
    loudness = 1.0
    for position, shards_of in split:
        steps = jax.random.uniform(jax.random.fold_in(jax.random.fold_in(stream_key, 6), position), (shards_of,), jnp.float32, least / len(split), top_value / len(split))
        loudness = loudness * jnp.repeat(jnp.exp(steps), extent[position] // shards_of).reshape((-1,) + (1,) * (len(extent) - 1 - position))
    return loudness


def centred(stream_key, shape, deviation, limit, shards=(), kind=jnp.bfloat16):
    entries = jax.random.normal(stream_key, shape, jnp.float32) * deviation
    if len(shards) > 0:
        entries = block_levels(stream_key, shape, shards, -0.22, 0.18) * entries
    return jnp.clip(entries, min=-limit, max=limit).astype(kind)


def setup_inputs(seed: int = 0) -> dict:
    streams_of = jax.random.split(jax.random.key(seed), 5)
    return {
        "queries": draw_queries(jax.random.fold_in(streams_of[4], 71), 0),
        "cache_keys": centred(streams_of[1], (HEADS, NK, D), 1.0, 6.0, ((1, 16),)),
        "cache_values": centred(streams_of[2], (HEADS, NK, D), 1.0, 6.0, ((1, 16),)),
        "selected": draw_selected(jax.random.fold_in(streams_of[4], 71), 0),
    }


ridge_weight = 0.1
theta_mid = 1.1
delta_half = 1.0


def reference(queries, cache_keys, cache_values, selected):
    score_scale = D ** -0.5
    key_float = cache_keys.astype(jnp.float32)
    value_float = cache_values.astype(jnp.float32)
    chosen = jnp.take_along_axis(key_float, selected[:, :, None].astype(jnp.int32), axis=1)
    block_rows = math.gcd(512, NQ)
    block_count = NQ // block_rows
    query_blocks = queries.astype(jnp.float32).reshape(HEADS, block_count, block_rows, D).transpose(1, 0, 2, 3)
    high = lax.Precision.HIGHEST

    def one_block(accumulated, query_block):
        gram_sum, rhs_sum = accumulated
        scores = jnp.einsum("hqd,hkd->hqk", query_block, key_float, precision=high) * score_scale
        peak = jnp.max(scores, axis=-1, keepdims=True)
        weights = jnp.exp(scores - peak)
        denominator = jnp.sum(weights, axis=-1, keepdims=True)
        numer = jnp.einsum("hqk,hkd->hqd", weights, value_float, precision=high)
        attended = (numer / denominator).astype(jnp.bfloat16)
        attended = lax.optimization_barrier(attended).astype(jnp.float32)
        compact = jnp.einsum("hqd,hkd->hqk", query_block, chosen, precision=high) * score_scale
        compact_peak = jnp.max(compact, axis=-1, keepdims=True)
        compact_w = jnp.exp(compact - compact_peak)
        probs = (compact_w / jnp.sum(compact_w, axis=-1, keepdims=True)).astype(jnp.bfloat16)
        probs = lax.optimization_barrier(probs).astype(jnp.float32)
        gram_sum = gram_sum + jnp.einsum("hqa,hqb->hab", probs, probs, precision=high)
        rhs_sum = rhs_sum + jnp.einsum("hqa,hqd->had", probs, attended, precision=high)
        return (gram_sum, rhs_sum), None

    start = (jnp.zeros((HEADS, M, M), jnp.float32), jnp.zeros((HEADS, M, D), jnp.float32))
    (gram_sum, rhs_sum), _ = lax.scan(one_block, start, query_blocks)
    weighting = M / NQ
    gram = gram_sum * weighting + ridge_weight * jnp.eye(M, dtype=jnp.float32)[None]
    rhs = rhs_sum * weighting
    sigma = theta_mid / delta_half
    solution = jnp.zeros_like(rhs)
    resid = rhs
    direction = rhs / theta_mid
    recur_now = 1.0 / sigma
    for iteration in range(STEPS):
        solution = solution + direction
        resid = resid - jnp.einsum("hab,hbd->had", gram, direction, precision=high)
        recur_next = 1.0 / (2.0 * sigma - recur_now)
        direction = recur_next * recur_now * direction + (2.0 * recur_next / delta_half) * resid
        recur_now = recur_next
    return solution, resid
```

```python
import jax
import jax.numpy as jnp
from jax import lax
from jax.sharding import PartitionSpec as P

STEPS = 3


ridge_weight = 0.1
theta_mid = 1.1
delta_half = 1.0

F32 = jnp.float32
BF16 = jnp.bfloat16


def exchange(tree, axis, bit):
    size = lax.axis_size(axis)
    pairs = [(s, s ^ bit) for s in range(size)]
    return jax.tree.map(lambda a: lax.ppermute(a, axis, pairs), tree)


def butterfly_sum(value, axis):
    bit = 1
    while bit < lax.axis_size(axis):
        value = value + exchange(value, axis, bit)
        bit *= 2
    return value


def butterfly(tree, axis, combine):
    bit = 1
    while bit < lax.axis_size(axis):
        tree = combine(tree, exchange(tree, axis, bit))
        bit *= 2
    return tree


def scatter_halving(blocks, axis):
    me = lax.axis_index(axis)
    bit = 1
    level = 0
    while bit < lax.axis_size(axis):
        rest = blocks.shape[0] // 2
        pair = blocks.reshape((rest, 2) + blocks.shape[1:])
        mine = (me >> level) & 1
        keep = jnp.where(mine == 0, pair[:, 0], pair[:, 1])
        give = jnp.where(mine == 0, pair[:, 1], pair[:, 0])
        blocks = keep + exchange(give, axis, bit)
        bit *= 2
        level += 1
    return blocks[0]


def split_dot(spec, low, wide):
    high = wide.astype(BF16)
    rest = (wide - high.astype(F32)).astype(BF16)
    return jnp.einsum(spec, low, high, preferred_element_type=F32) + jnp.einsum(
        spec, low, rest, preferred_element_type=F32
    )


def combine_stats(first, second):
    peak_a, denom_a, numer_a, cpeak_a, cdenom_a = first
    peak_b, denom_b, numer_b, cpeak_b, cdenom_b = second
    peak = jnp.maximum(peak_a, peak_b)
    fa = jnp.exp(peak_a - peak)
    fb = jnp.exp(peak_b - peak)
    cpeak = jnp.maximum(cpeak_a, cpeak_b)
    ga = jnp.exp(cpeak_a - cpeak)
    gb = jnp.exp(cpeak_b - cpeak)
    return (
        peak,
        denom_a * fa + denom_b * fb,
        numer_a * fa[..., None] + numer_b * fb[..., None],
        cpeak,
        cdenom_a * ga + cdenom_b * gb,
    )


def per_device(queries, cache_keys, cache_values, selected):
    head_count, query_rows, head_width = queries.shape
    key_rows = cache_keys.shape[1]
    order_size = selected.shape[1]
    row_devices = lax.axis_size("pb")
    col_devices = lax.axis_size("kv")
    col_len = order_size // col_devices
    score_scale = head_width ** (-0.5)
    me_kv = lax.axis_index("kv")

    local_pos = me_kv * key_rows + jnp.arange(key_rows, dtype=jnp.int32)
    owned = selected[:, :, None] == local_pos[None, None, :]
    picked = jnp.einsum(
        "hak,hkd->had", owned.astype(BF16), cache_keys, preferred_element_type=F32
    ).astype(BF16)
    kept_mask = jnp.any(owned, axis=1)
    blocks = picked.reshape(head_count, col_devices, col_len, head_width).transpose(1, 0, 2, 3)
    chosen_block = scatter_halving(blocks, "kv")

    scores = (
        jnp.einsum("hqd,hkd->hqk", queries, cache_keys, preferred_element_type=F32) * score_scale
    )
    peak = jnp.max(scores, axis=-1)
    weights = jnp.exp(scores - peak[..., None])
    denom = jnp.sum(weights, axis=-1)
    w_high = weights.astype(BF16)
    w_low = (weights - w_high.astype(F32)).astype(BF16)
    numer = jnp.einsum(
        "hqk,hkd->hqd", w_high, cache_values, preferred_element_type=F32
    ) + jnp.einsum("hqk,hkd->hqd", w_low, cache_values, preferred_element_type=F32)
    floor = jnp.float32(-1e30)
    kept_scores = jnp.where(kept_mask[:, None, :], scores, floor)
    cpeak = jnp.max(kept_scores, axis=-1)
    cweights = jnp.where(kept_mask[:, None, :], jnp.exp(kept_scores - cpeak[..., None]), 0.0)
    cdenom = jnp.sum(cweights, axis=-1)

    peak, denom, numer, cpeak, cdenom = butterfly(
        (peak, denom, numer, cpeak, cdenom), "kv", combine_stats
    )
    attended = (numer / denom[..., None]).astype(BF16)

    compact = (
        jnp.einsum("hqd,hkd->hqk", queries, chosen_block, preferred_element_type=F32)
        * score_scale
    )
    probs = (jnp.exp(compact - cpeak[..., None]) / cdenom[..., None]).astype(BF16)

    weighting = order_size / (query_rows * row_devices)
    rhs_part = jnp.einsum("hqa,hqd->had", probs, attended, preferred_element_type=F32)
    rhs = butterfly_sum(rhs_part, "pb") * weighting

    def gram_times(vec):
        across = butterfly_sum(split_dot("hqa,had->hqd", probs, vec), "kv")
        back = butterfly_sum(split_dot("hqa,hqd->had", probs, across), "pb")
        return back * weighting + ridge_weight * vec

    sigma = theta_mid / delta_half
    solution = jnp.zeros_like(rhs)
    resid = rhs
    direction = rhs / theta_mid
    recur_now = 1.0 / sigma
    for iteration in range(STEPS):
        solution = solution + direction
        resid = resid - gram_times(direction)
        recur_next = 1.0 / (2.0 * sigma - recur_now)
        direction = recur_next * recur_now * direction + 2.0 * recur_next / delta_half * resid
        recur_now = recur_next
    return (solution, resid)


def solution(mesh):
    in_specs = (P(None, "pb", None), P(None, "kv", None), P(None, "kv", None), P())
    out_specs = (P(None, "kv", None), P(None, "kv", None))
    return jax.shard_map(
        per_device, mesh=mesh, in_specs=in_specs, out_specs=out_specs, check_vma=False
    )
```

```python
import jax
import jax.numpy as jnp
from jax import lax
from jax.sharding import PartitionSpec as P

STEPS = 3


ridge_weight = 0.1
theta_mid = 1.1
delta_half = 1.0

F32 = jnp.float32
BF16 = jnp.bfloat16


def digit_groups(size):
    groups = []
    bit = 1
    while bit < size:
        radix = 4 if bit * 4 <= size else 2
        groups.append((bit, radix))
        bit *= radix
    return groups


def gather_group(value, axis, stride, radix):
    size = lax.axis_size(axis)
    me = lax.axis_index(axis)
    digit = (me // stride) % radix
    got = [value]
    for k in range(1, radix):
        pairs = [(s, s ^ (k * stride)) for s in range(size)]
        got.append(jax.tree.map(lambda a: lax.ppermute(a, axis, pairs), value))
    stacked = jax.tree.map(lambda *a: jnp.stack(a), *got)
    return [
        jax.tree.map(lambda a: lax.dynamic_index_in_dim(a, digit ^ g, 0, False), stacked)
        for g in range(radix)
    ]


def group_sum(value, axis):
    for stride, radix in digit_groups(lax.axis_size(axis)):
        members = gather_group(value, axis, stride, radix)
        value = members[0]
        for other in members[1:]:
            value = value + other
    return value


def scatter_groups(blocks, axis):
    size = lax.axis_size(axis)
    me = lax.axis_index(axis)
    for stride, radix in digit_groups(size):
        digit = (me // stride) % radix
        rest = blocks.shape[0] // radix
        split = blocks.reshape((rest, radix) + blocks.shape[1:])
        total = lax.dynamic_index_in_dim(split, digit, 1, False)
        for k in range(1, radix):
            pairs = [(s, s ^ (k * stride)) for s in range(size)]
            give = lax.dynamic_index_in_dim(split, digit ^ k, 1, False)
            total = total + lax.ppermute(give, axis, pairs)
        blocks = total
    return blocks[0]


def split_dot(spec, low, wide):
    high = wide.astype(BF16)
    rest = (wide - high.astype(F32)).astype(BF16)
    return jnp.einsum(spec, low, high, preferred_element_type=F32) + jnp.einsum(
        spec, low, rest, preferred_element_type=F32
    )


def combine_members(members, rows):
    def unpack(a):
        stats = a[:, rows:, :].reshape(a.shape[0], 4, rows)
        return a[:, :rows, :], stats[:, 0], stats[:, 1], stats[:, 2], stats[:, 3]

    parts = [unpack(a) for a in members]
    peak = parts[0][1]
    cpeak = parts[0][3]
    for p in parts[1:]:
        peak = jnp.maximum(peak, p[1])
        cpeak = jnp.maximum(cpeak, p[3])
    numer = denom = cdenom = None
    for p in parts:
        f = jnp.exp(p[1] - peak)
        g = jnp.exp(p[3] - cpeak)
        n_term = p[0] * f[..., None]
        numer = n_term if numer is None else numer + n_term
        denom = p[2] * f if denom is None else denom + p[2] * f
        cdenom = p[4] * g if cdenom is None else cdenom + p[4] * g
    return numer, peak, denom, cpeak, cdenom


def pack(numer, peak, denom, cpeak, cdenom):
    heads, rows, width = numer.shape
    stats = jnp.stack([peak, denom, cpeak, cdenom], axis=1).reshape(heads, 4 * rows // width, width)
    return jnp.concatenate([numer, stats], axis=1)


def per_device(queries, cache_keys, cache_values, selected):
    head_count, query_rows, head_width = queries.shape
    key_rows = cache_keys.shape[1]
    order_size = selected.shape[1]
    row_devices = lax.axis_size("pb")
    col_devices = lax.axis_size("kv")
    col_len = order_size // col_devices
    score_scale = head_width ** (-0.5)
    me_kv = lax.axis_index("kv")

    local_pos = me_kv * key_rows + jnp.arange(key_rows, dtype=jnp.int32)
    owned = selected[:, :, None] == local_pos[None, None, :]
    picked = jnp.einsum(
        "hak,hkd->had", owned.astype(BF16), cache_keys, preferred_element_type=F32
    ).astype(BF16)
    kept_mask = jnp.any(owned, axis=1)
    blocks = picked.reshape(head_count, col_devices, col_len, head_width).transpose(1, 0, 2, 3)
    chosen_block = scatter_groups(blocks, "kv")

    scores = (
        jnp.einsum("hqd,hkd->hqk", queries, cache_keys, preferred_element_type=F32) * score_scale
    )
    peak = jnp.max(scores, axis=-1)
    weights = jnp.exp(scores - peak[..., None])
    denom = jnp.sum(weights, axis=-1)
    w_high = weights.astype(BF16)
    w_low = (weights - w_high.astype(F32)).astype(BF16)
    numer = jnp.einsum(
        "hqk,hkd->hqd", w_high, cache_values, preferred_element_type=F32
    ) + jnp.einsum("hqk,hkd->hqd", w_low, cache_values, preferred_element_type=F32)
    floor = jnp.float32(-1e30)
    kept_scores = jnp.where(kept_mask[:, None, :], scores, floor)
    cpeak = jnp.max(kept_scores, axis=-1)
    cweights = jnp.where(kept_mask[:, None, :], jnp.exp(kept_scores - cpeak[..., None]), 0.0)
    cdenom = jnp.sum(cweights, axis=-1)

    packed = pack(numer, peak, denom, cpeak, cdenom)
    for stride, radix in digit_groups(col_devices):
        members = gather_group(packed, "kv", stride, radix)
        numer, peak, denom, cpeak, cdenom = combine_members(members, query_rows)
        packed = pack(numer, peak, denom, cpeak, cdenom)
    attended = (numer / denom[..., None]).astype(BF16)

    compact = (
        jnp.einsum("hqd,hkd->hqk", queries, chosen_block, preferred_element_type=F32)
        * score_scale
    )
    probs = (jnp.exp(compact - cpeak[..., None]) / cdenom[..., None]).astype(BF16)

    weighting = order_size / (query_rows * row_devices)
    rhs_part = jnp.einsum("hqa,hqd->had", probs, attended, preferred_element_type=F32)
    rhs = group_sum(rhs_part, "pb") * weighting

    def gram_times(vec):
        across = group_sum(split_dot("hqa,had->hqd", probs, vec), "kv")
        back = group_sum(split_dot("hqa,hqd->had", probs, across), "pb")
        return back * weighting + ridge_weight * vec

    sigma = theta_mid / delta_half
    solution = jnp.zeros_like(rhs)
    resid = rhs
    direction = rhs / theta_mid
    recur_now = 1.0 / sigma
    for iteration in range(STEPS):
        solution = solution + direction
        resid = resid - gram_times(direction)
        recur_next = 1.0 / (2.0 * sigma - recur_now)
        direction = recur_next * recur_now * direction + 2.0 * recur_next / delta_half * resid
        recur_now = recur_next
    return (solution, resid)


def solution(mesh):
    in_specs = (P(None, "pb", None), P(None, "kv", None), P(None, "kv", None), P())
    out_specs = (P(None, "kv", None), P(None, "kv", None))
    return jax.shard_map(
        per_device, mesh=mesh, in_specs=in_specs, out_specs=out_specs, check_vma=False
    )
```

```python
import jax
import jax.numpy as jnp
from jax import lax
from jax.sharding import PartitionSpec as P

STEPS = 3


ridge_weight = 0.1
theta_mid = 1.1
delta_half = 1.0

F32 = jnp.float32
BF16 = jnp.bfloat16


def digit_groups(size):
    groups = []
    bit = 1
    while bit < size:
        radix = 4 if bit * 4 <= size else 2
        groups.append((bit, radix))
        bit *= radix
    return groups


def gather_group(value, axis, stride, radix):
    size = lax.axis_size(axis)
    me = lax.axis_index(axis)
    digit = (me // stride) % radix
    got = [value]
    for k in range(1, radix):
        pairs = [(s, s ^ (k * stride)) for s in range(size)]
        got.append(jax.tree.map(lambda a: lax.ppermute(a, axis, pairs), value))
    stacked = jax.tree.map(lambda *a: jnp.stack(a), *got)
    return [
        jax.tree.map(lambda a: lax.dynamic_index_in_dim(a, digit ^ g, 0, False), stacked)
        for g in range(radix)
    ]


def group_sum(value, axis):
    for stride, radix in digit_groups(lax.axis_size(axis)):
        members = gather_group(value, axis, stride, radix)
        value = members[0]
        for other in members[1:]:
            value = value + other
    return value


def scatter_groups(blocks, axis):
    size = lax.axis_size(axis)
    me = lax.axis_index(axis)
    for stride, radix in digit_groups(size):
        digit = (me // stride) % radix
        rest = blocks.shape[0] // radix
        split = blocks.reshape((rest, radix) + blocks.shape[1:])
        total = lax.dynamic_index_in_dim(split, digit, 1, False)
        for k in range(1, radix):
            pairs = [(s, s ^ (k * stride)) for s in range(size)]
            give = lax.dynamic_index_in_dim(split, digit ^ k, 1, False)
            total = total + lax.ppermute(give, axis, pairs)
        blocks = total
    return blocks[0]


def split_dot(spec, low, wide):
    high = wide.astype(BF16)
    rest = (wide - high.astype(F32)).astype(BF16)
    return jnp.einsum(spec, low, high, preferred_element_type=F32) + jnp.einsum(
        spec, low, rest, preferred_element_type=F32
    )


def combine_members(members, rows):
    def unpack(a):
        stats = a[:, rows:, :].reshape(a.shape[0], 4, rows)
        return a[:, :rows, :], stats[:, 0], stats[:, 1], stats[:, 2], stats[:, 3]

    parts = [unpack(a) for a in members]
    peak = parts[0][1]
    cpeak = parts[0][3]
    for p in parts[1:]:
        peak = jnp.maximum(peak, p[1])
        cpeak = jnp.maximum(cpeak, p[3])
    numer = denom = cdenom = None
    for p in parts:
        f = jnp.exp(p[1] - peak)
        g = jnp.exp(p[3] - cpeak)
        n_term = p[0] * f[..., None]
        numer = n_term if numer is None else numer + n_term
        denom = p[2] * f if denom is None else denom + p[2] * f
        cdenom = p[4] * g if cdenom is None else cdenom + p[4] * g
    return numer, peak, denom, cpeak, cdenom


def pack(numer, peak, denom, cpeak, cdenom):
    heads, rows, width = numer.shape
    stats = jnp.stack([peak, denom, cpeak, cdenom], axis=1).reshape(heads, 4 * rows // width, width)
    return jnp.concatenate([numer, stats], axis=1)


def per_device(queries, cache_keys, cache_values, selected):
    head_count, query_rows, head_width = queries.shape
    key_rows = cache_keys.shape[1]
    order_size = selected.shape[1]
    row_devices = lax.axis_size("pb")
    col_devices = lax.axis_size("kv")
    col_len = order_size // col_devices
    score_scale = head_width ** (-0.5)
    me_kv = lax.axis_index("kv")

    local_pos = me_kv * key_rows + jnp.arange(key_rows, dtype=jnp.int32)
    owned = selected[:, :, None] == local_pos[None, None, :]
    picked = jnp.einsum(
        "hak,hkd->had", owned.astype(BF16), cache_keys, preferred_element_type=F32
    ).astype(BF16)
    kept_mask = jnp.any(owned, axis=1)
    blocks = picked.reshape(head_count, col_devices, col_len, head_width).transpose(1, 0, 2, 3)
    chosen_block = scatter_groups(blocks, "kv")

    scores = (
        jnp.einsum("hqd,hkd->hqk", queries, cache_keys, preferred_element_type=F32) * score_scale
    )
    peak = jnp.max(scores, axis=-1)
    weights = jnp.exp(scores - peak[..., None])
    denom = jnp.sum(weights, axis=-1)
    w_high = weights.astype(BF16)
    w_low = (weights - w_high.astype(F32)).astype(BF16)
    numer = jnp.einsum(
        "hqk,hkd->hqd", w_high, cache_values, preferred_element_type=F32
    ) + jnp.einsum("hqk,hkd->hqd", w_low, cache_values, preferred_element_type=F32)
    floor = jnp.float32(-1e30)
    kept_scores = jnp.where(kept_mask[:, None, :], scores, floor)
    cpeak = jnp.max(kept_scores, axis=-1)
    cweights = jnp.where(kept_mask[:, None, :], jnp.exp(kept_scores - cpeak[..., None]), 0.0)
    cdenom = jnp.sum(cweights, axis=-1)

    packed = pack(numer, peak, denom, cpeak, cdenom)
    for stride, radix in digit_groups(col_devices):
        members = gather_group(packed, "kv", stride, radix)
        numer, peak, denom, cpeak, cdenom = combine_members(members, query_rows)
        packed = pack(numer, peak, denom, cpeak, cdenom)
    attended = (numer / denom[..., None]).astype(BF16)

    compact = (
        jnp.einsum("hqd,hkd->hqk", queries, chosen_block, preferred_element_type=F32)
        * score_scale
    )
    probs = (jnp.exp(compact - cpeak[..., None]) / cdenom[..., None]).astype(BF16)

    weighting = order_size / (query_rows * row_devices)
    rhs_part = jnp.einsum("hqa,hqd->had", probs, attended, preferred_element_type=F32)
    sigma = theta_mid / delta_half
    outputs = []
    for head in range(head_count):
        head_probs = probs[head : head + 1]

        def gram_times(vec):
            across = group_sum(split_dot("hqa,had->hqd", head_probs, vec), "kv")
            back = group_sum(split_dot("hqa,hqd->had", head_probs, across), "pb")
            return back * weighting + ridge_weight * vec

        rhs = group_sum(rhs_part[head : head + 1], "pb") * weighting
        solution = jnp.zeros_like(rhs)
        resid = rhs
        direction = rhs / theta_mid
        recur_now = 1.0 / sigma
        for iteration in range(STEPS):
            solution = solution + direction
            resid = resid - gram_times(direction)
            recur_next = 1.0 / (2.0 * sigma - recur_now)
            direction = recur_next * recur_now * direction + 2.0 * recur_next / delta_half * resid
            recur_now = recur_next
        outputs.append((solution, resid))
    solution = jnp.concatenate([o[0] for o in outputs], axis=0)
    resid = jnp.concatenate([o[1] for o in outputs], axis=0)
    return (solution, resid)


def solution(mesh):
    in_specs = (P(None, "pb", None), P(None, "kv", None), P(None, "kv", None), P())
    out_specs = (P(None, "kv", None), P(None, "kv", None))
    return jax.shard_map(
        per_device, mesh=mesh, in_specs=in_specs, out_specs=out_specs, check_vma=False
    )
```

```python
import jax
import jax.numpy as jnp
from jax import lax
from jax.sharding import PartitionSpec as P

STEPS = 3


ridge_weight = 0.1
theta_mid = 1.1
delta_half = 1.0

F32 = jnp.float32
BF16 = jnp.bfloat16


def digit_groups(size):
    groups = []
    bit = 1
    while bit < size:
        radix = 4 if bit * 4 <= size else 2
        groups.append((bit, radix))
        bit *= radix
    return groups


def gather_group(value, axis, stride, radix):
    size = lax.axis_size(axis)
    me = lax.axis_index(axis)
    digit = (me // stride) % radix
    got = [value]
    for k in range(1, radix):
        pairs = [(s, s ^ (k * stride)) for s in range(size)]
        got.append(jax.tree.map(lambda a: lax.ppermute(a, axis, pairs), value))
    stacked = jax.tree.map(lambda *a: jnp.stack(a), *got)
    return [
        jax.tree.map(lambda a: lax.dynamic_index_in_dim(a, digit ^ g, 0, False), stacked)
        for g in range(radix)
    ]


def gather_bits(value, axis, bits):
    size = lax.axis_size(axis)
    me = lax.axis_index(axis)
    digit = sum(((me >> b) & 1) << t for t, b in enumerate(bits))
    radix = 1 << len(bits)
    got = [value]
    for k in range(1, radix):
        mask = sum(((k >> t) & 1) << b for t, b in enumerate(bits))
        pairs = [(s, s ^ mask) for s in range(size)]
        got.append(lax.ppermute(value, axis, pairs))
    stacked = jnp.stack(got)
    return [lax.dynamic_index_in_dim(stacked, digit ^ g, 0, False) for g in range(radix)]


def bit_stages(size):
    count = size.bit_length() - 1
    if count == 5:
        return [[0, 1], [3, 4], [2]]
    return [[b, b + 1] if b + 1 < count else [b] for b in range(0, count, 2)]


def group_sum(value, axis):
    for bits in bit_stages(lax.axis_size(axis)):
        members = gather_bits(value, axis, bits)
        value = members[0]
        for other in members[1:]:
            value = value + other
    return value


def scatter_groups(blocks, axis):
    size = lax.axis_size(axis)
    me = lax.axis_index(axis)
    for stride, radix in digit_groups(size):
        digit = (me // stride) % radix
        rest = blocks.shape[0] // radix
        split = blocks.reshape((rest, radix) + blocks.shape[1:])
        total = lax.dynamic_index_in_dim(split, digit, 1, False)
        for k in range(1, radix):
            pairs = [(s, s ^ (k * stride)) for s in range(size)]
            give = lax.dynamic_index_in_dim(split, digit ^ k, 1, False)
            total = total + lax.ppermute(give, axis, pairs)
        blocks = total
    return blocks[0]


def split_dot(spec, low, wide):
    high = wide.astype(BF16)
    rest = (wide - high.astype(F32)).astype(BF16)
    return jnp.einsum(spec, low, high, preferred_element_type=F32) + jnp.einsum(
        spec, low, rest, preferred_element_type=F32
    )


def combine_members(members, rows):
    def unpack(a):
        stats = a[:, rows:, :].reshape(a.shape[0], 4, rows)
        return a[:, :rows, :], stats[:, 0], stats[:, 1], stats[:, 2], stats[:, 3]

    parts = [unpack(a) for a in members]
    peak = parts[0][1]
    cpeak = parts[0][3]
    for p in parts[1:]:
        peak = jnp.maximum(peak, p[1])
        cpeak = jnp.maximum(cpeak, p[3])
    numer = denom = cdenom = None
    for p in parts:
        f = jnp.exp(p[1] - peak)
        g = jnp.exp(p[3] - cpeak)
        n_term = p[0] * f[..., None]
        numer = n_term if numer is None else numer + n_term
        denom = p[2] * f if denom is None else denom + p[2] * f
        cdenom = p[4] * g if cdenom is None else cdenom + p[4] * g
    return numer, peak, denom, cpeak, cdenom


def pack(numer, peak, denom, cpeak, cdenom):
    heads, rows, width = numer.shape
    stats = jnp.stack([peak, denom, cpeak, cdenom], axis=1).reshape(heads, 4 * rows // width, width)
    return jnp.concatenate([numer, stats], axis=1)


def per_device(queries, cache_keys, cache_values, selected):
    head_count, query_rows, head_width = queries.shape
    key_rows = cache_keys.shape[1]
    order_size = selected.shape[1]
    row_devices = lax.axis_size("pb")
    col_devices = lax.axis_size("kv")
    col_len = order_size // col_devices
    score_scale = head_width ** (-0.5)
    me_kv = lax.axis_index("kv")

    local_pos = me_kv * key_rows + jnp.arange(key_rows, dtype=jnp.int32)
    owned = selected[:, :, None] == local_pos[None, None, :]
    picked = jnp.einsum(
        "hak,hkd->had", owned.astype(BF16), cache_keys, preferred_element_type=F32
    ).astype(BF16)
    kept_mask = jnp.any(owned, axis=1)
    blocks = picked.reshape(head_count, col_devices, col_len, head_width).transpose(1, 0, 2, 3)

    scores = (
        jnp.einsum("hqd,hkd->hqk", queries, cache_keys, preferred_element_type=F32) * score_scale
    )
    peak = jnp.max(scores, axis=-1)
    weights = jnp.exp(scores - peak[..., None])
    denom = jnp.sum(weights, axis=-1)
    w_high = weights.astype(BF16)
    w_low = (weights - w_high.astype(F32)).astype(BF16)
    numer = jnp.einsum(
        "hqk,hkd->hqd", w_high, cache_values, preferred_element_type=F32
    ) + jnp.einsum("hqk,hkd->hqd", w_low, cache_values, preferred_element_type=F32)
    floor = jnp.float32(-1e30)
    kept_scores = jnp.where(kept_mask[:, None, :], scores, floor)
    cpeak = jnp.max(kept_scores, axis=-1)
    cweights = jnp.where(kept_mask[:, None, :], jnp.exp(kept_scores - cpeak[..., None]), 0.0)
    cdenom = jnp.sum(cweights, axis=-1)

    packed = pack(numer, peak, denom, cpeak, cdenom)
    for stride, radix in digit_groups(col_devices):
        digit = (me_kv // stride) % radix
        split = blocks.reshape((blocks.shape[0] // radix, radix) + blocks.shape[1:])
        total = lax.dynamic_index_in_dim(split, digit, 1, False)
        got = [packed]
        for k in range(1, radix):
            pairs = [(s, s ^ (k * stride)) for s in range(col_devices)]
            give = lax.dynamic_index_in_dim(split, digit ^ k, 1, False)
            key_rows_sent = give.size // head_width
            payload = jnp.concatenate(
                [give.astype(F32).reshape(key_rows_sent, head_width), packed.reshape(-1, head_width)]
            )
            arrived = lax.ppermute(payload, "kv", pairs)
            total = total + arrived[:key_rows_sent].reshape(give.shape).astype(BF16)
            got.append(arrived[key_rows_sent:].reshape(packed.shape))
        blocks = total
        stacked = jnp.stack(got)
        members = [lax.dynamic_index_in_dim(stacked, digit ^ g, 0, False) for g in range(radix)]
        numer, peak, denom, cpeak, cdenom = combine_members(members, query_rows)
        packed = pack(numer, peak, denom, cpeak, cdenom)
    chosen_block = blocks[0]
    attended = (numer / denom[..., None]).astype(BF16)

    compact = (
        jnp.einsum("hqd,hkd->hqk", queries, chosen_block, preferred_element_type=F32)
        * score_scale
    )
    probs = (jnp.exp(compact - cpeak[..., None]) / cdenom[..., None]).astype(BF16)

    weighting = order_size / (query_rows * row_devices)
    rhs_part = jnp.einsum("hqa,hqd->had", probs, attended, preferred_element_type=F32)
    rhs = group_sum(rhs_part, "pb") * weighting

    def gram_times(vec):
        across = group_sum(split_dot("hqa,had->hqd", probs, vec), "kv")
        back = group_sum(split_dot("hqa,hqd->had", probs, across), "pb")
        return back * weighting + ridge_weight * vec

    sigma = theta_mid / delta_half
    solution = jnp.zeros_like(rhs)
    resid = rhs
    direction = rhs / theta_mid
    recur_now = 1.0 / sigma
    for iteration in range(STEPS):
        solution = solution + direction
        resid = resid - gram_times(direction)
        recur_next = 1.0 / (2.0 * sigma - recur_now)
        direction = recur_next * recur_now * direction + 2.0 * recur_next / delta_half * resid
        recur_now = recur_next
    return (solution, resid)


def solution(mesh):
    in_specs = (P(None, "pb", None), P(None, "kv", None), P(None, "kv", None), P())
    out_specs = (P(None, "kv", None), P(None, "kv", None))
    return jax.shard_map(
        per_device, mesh=mesh, in_specs=in_specs, out_specs=out_specs, check_vma=False
    )
```

```python
import jax
import jax.numpy as jnp
from jax import lax
from jax.sharding import PartitionSpec as P

STEPS = 3


ridge_weight = 0.1
theta_mid = 1.1
delta_half = 1.0

F32 = jnp.float32
BF16 = jnp.bfloat16


def digit_groups(size):
    groups = []
    bit = 1
    while bit < size:
        radix = 4 if bit * 4 <= size else 2
        groups.append((bit, radix))
        bit *= radix
    return groups


def gather_group(value, axis, stride, radix):
    size = lax.axis_size(axis)
    me = lax.axis_index(axis)
    digit = (me // stride) % radix
    got = [value]
    for k in range(1, radix):
        pairs = [(s, s ^ (k * stride)) for s in range(size)]
        got.append(jax.tree.map(lambda a: lax.ppermute(a, axis, pairs), value))
    stacked = jax.tree.map(lambda *a: jnp.stack(a), *got)
    return [
        jax.tree.map(lambda a: lax.dynamic_index_in_dim(a, digit ^ g, 0, False), stacked)
        for g in range(radix)
    ]


def gather_bits(value, axis, bits):
    size = lax.axis_size(axis)
    me = lax.axis_index(axis)
    digit = sum(((me >> b) & 1) << t for t, b in enumerate(bits))
    radix = 1 << len(bits)
    got = [value]
    for k in range(1, radix):
        mask = sum(((k >> t) & 1) << b for t, b in enumerate(bits))
        pairs = [(s, s ^ mask) for s in range(size)]
        got.append(lax.ppermute(value, axis, pairs))
    stacked = jnp.stack(got)
    return [lax.dynamic_index_in_dim(stacked, digit ^ g, 0, False) for g in range(radix)]


def sum_over_bits(value, axis, stages):
    for bits in stages:
        members = gather_bits(value, axis, bits)
        value = members[0]
        for other in members[1:]:
            value = value + other
    return value


def bit_stages(bits):
    return [bits[b : b + 2] for b in range(0, len(bits), 2)]


def group_sum(value, axis):
    count = lax.axis_size(axis).bit_length() - 1
    if count == 5:
        return sum_over_bits(value, axis, [[0, 1], [3, 4], [2]])
    return sum_over_bits(value, axis, bit_stages(list(range(count))))


def pair_split_sum(value, axis, split_axis):
    count = lax.axis_size(axis).bit_length() - 1
    value = sum_over_bits(value, axis, [[0]])
    half = value.shape[split_axis] // 2
    low = (lax.axis_index(axis) & 1) == 0
    first = lax.slice_in_dim(value, 0, half, axis=split_axis)
    second = lax.slice_in_dim(value, half, 2 * half, axis=split_axis)
    mine = jnp.where(low, first, second)
    mine = sum_over_bits(mine, axis, bit_stages(list(range(1, count))))
    other = lax.ppermute(
        mine, axis, [(s, s ^ 1) for s in range(lax.axis_size(axis))]
    )
    return jnp.concatenate(
        [jnp.where(low, mine, other), jnp.where(low, other, mine)], axis=split_axis
    )


def scatter_groups(blocks, axis):
    size = lax.axis_size(axis)
    me = lax.axis_index(axis)
    for stride, radix in digit_groups(size):
        digit = (me // stride) % radix
        rest = blocks.shape[0] // radix
        split = blocks.reshape((rest, radix) + blocks.shape[1:])
        total = lax.dynamic_index_in_dim(split, digit, 1, False)
        for k in range(1, radix):
            pairs = [(s, s ^ (k * stride)) for s in range(size)]
            give = lax.dynamic_index_in_dim(split, digit ^ k, 1, False)
            total = total + lax.ppermute(give, axis, pairs)
        blocks = total
    return blocks[0]


def split_dot(spec, low, wide):
    high = wide.astype(BF16)
    rest = (wide - high.astype(F32)).astype(BF16)
    return jnp.einsum(spec, low, high, preferred_element_type=F32) + jnp.einsum(
        spec, low, rest, preferred_element_type=F32
    )


def combine_members(members, rows):
    def unpack(a):
        stats = a[:, rows:, :].reshape(a.shape[0], 4, rows)
        return a[:, :rows, :], stats[:, 0], stats[:, 1], stats[:, 2], stats[:, 3]

    parts = [unpack(a) for a in members]
    peak = parts[0][1]
    cpeak = parts[0][3]
    for p in parts[1:]:
        peak = jnp.maximum(peak, p[1])
        cpeak = jnp.maximum(cpeak, p[3])
    numer = denom = cdenom = None
    for p in parts:
        f = jnp.exp(p[1] - peak)
        g = jnp.exp(p[3] - cpeak)
        n_term = p[0] * f[..., None]
        numer = n_term if numer is None else numer + n_term
        denom = p[2] * f if denom is None else denom + p[2] * f
        cdenom = p[4] * g if cdenom is None else cdenom + p[4] * g
    return numer, peak, denom, cpeak, cdenom


def pack(numer, peak, denom, cpeak, cdenom):
    heads, rows, width = numer.shape
    stats = jnp.stack([peak, denom, cpeak, cdenom], axis=1).reshape(heads, 4 * rows // width, width)
    return jnp.concatenate([numer, stats], axis=1)


def per_device(queries, cache_keys, cache_values, selected):
    head_count, query_rows, head_width = queries.shape
    key_rows = cache_keys.shape[1]
    order_size = selected.shape[1]
    row_devices = lax.axis_size("pb")
    col_devices = lax.axis_size("kv")
    col_len = order_size // col_devices
    score_scale = head_width ** (-0.5)
    me_kv = lax.axis_index("kv")

    local_pos = me_kv * key_rows + jnp.arange(key_rows, dtype=jnp.int32)
    owned = selected[:, :, None] == local_pos[None, None, :]
    picked = jnp.einsum(
        "hak,hkd->had", owned.astype(BF16), cache_keys, preferred_element_type=F32
    ).astype(BF16)
    kept_mask = jnp.any(owned, axis=1)
    blocks = picked.reshape(head_count, col_devices, col_len, head_width).transpose(1, 0, 2, 3)
    chosen_block = scatter_groups(blocks, "kv")

    scores = (
        jnp.einsum("hqd,hkd->hqk", queries, cache_keys, preferred_element_type=F32) * score_scale
    )
    peak = jnp.max(scores, axis=-1)
    weights = jnp.exp(scores - peak[..., None])
    denom = jnp.sum(weights, axis=-1)
    w_high = weights.astype(BF16)
    w_low = (weights - w_high.astype(F32)).astype(BF16)
    numer = jnp.einsum(
        "hqk,hkd->hqd", w_high, cache_values, preferred_element_type=F32
    ) + jnp.einsum("hqk,hkd->hqd", w_low, cache_values, preferred_element_type=F32)
    floor = jnp.float32(-1e30)
    kept_scores = jnp.where(kept_mask[:, None, :], scores, floor)
    cpeak = jnp.max(kept_scores, axis=-1)
    cweights = jnp.where(kept_mask[:, None, :], jnp.exp(kept_scores - cpeak[..., None]), 0.0)
    cdenom = jnp.sum(cweights, axis=-1)

    packed = pack(numer, peak, denom, cpeak, cdenom)
    for stride, radix in digit_groups(col_devices):
        members = gather_group(packed, "kv", stride, radix)
        numer, peak, denom, cpeak, cdenom = combine_members(members, query_rows)
        packed = pack(numer, peak, denom, cpeak, cdenom)
    attended = (numer / denom[..., None]).astype(BF16)

    compact = (
        jnp.einsum("hqd,hkd->hqk", queries, chosen_block, preferred_element_type=F32)
        * score_scale
    )
    probs = (jnp.exp(compact - cpeak[..., None]) / cdenom[..., None]).astype(BF16)

    weighting = order_size / (query_rows * row_devices)
    rhs_part = jnp.einsum("hqa,hqd->had", probs, attended, preferred_element_type=F32)
    rhs = group_sum(rhs_part, "pb") * weighting

    def gram_times(vec):
        across = pair_split_sum(split_dot("hqa,had->hqd", probs, vec), "kv", 1)
        back = group_sum(split_dot("hqa,hqd->had", probs, across), "pb")
        return back * weighting + ridge_weight * vec

    sigma = theta_mid / delta_half
    solution = jnp.zeros_like(rhs)
    resid = rhs
    direction = rhs / theta_mid
    recur_now = 1.0 / sigma
    for iteration in range(STEPS):
        solution = solution + direction
        resid = resid - gram_times(direction)
        recur_next = 1.0 / (2.0 * sigma - recur_now)
        direction = recur_next * recur_now * direction + 2.0 * recur_next / delta_half * resid
        recur_now = recur_next
    return (solution, resid)


def solution(mesh):
    in_specs = (P(None, "pb", None), P(None, "kv", None), P(None, "kv", None), P())
    out_specs = (P(None, "kv", None), P(None, "kv", None))
    return jax.shard_map(
        per_device, mesh=mesh, in_specs=in_specs, out_specs=out_specs, check_vma=False
    )
```

```python
import jax
import jax.numpy as jnp
from jax import lax
from jax.sharding import PartitionSpec as P

STEPS = 3


ridge_weight = 0.1
theta_mid = 1.1
delta_half = 1.0

F32 = jnp.float32
BF16 = jnp.bfloat16


def digit_groups(size):
    groups = []
    bit = 1
    while bit < size:
        radix = 4 if bit * 4 <= size else 2
        groups.append((bit, radix))
        bit *= radix
    return groups


def gather_group(value, axis, stride, radix):
    size = lax.axis_size(axis)
    me = lax.axis_index(axis)
    digit = (me // stride) % radix
    got = [value]
    for k in range(1, radix):
        pairs = [(s, s ^ (k * stride)) for s in range(size)]
        got.append(jax.tree.map(lambda a: lax.ppermute(a, axis, pairs), value))
    stacked = jax.tree.map(lambda *a: jnp.stack(a), *got)
    return [
        jax.tree.map(lambda a: lax.dynamic_index_in_dim(a, digit ^ g, 0, False), stacked)
        for g in range(radix)
    ]


def gather_bits(value, axis, bits):
    size = lax.axis_size(axis)
    me = lax.axis_index(axis)
    digit = sum(((me >> b) & 1) << t for t, b in enumerate(bits))
    radix = 1 << len(bits)
    got = [value]
    for k in range(1, radix):
        mask = sum(((k >> t) & 1) << b for t, b in enumerate(bits))
        pairs = [(s, s ^ mask) for s in range(size)]
        got.append(lax.ppermute(value, axis, pairs))
    stacked = jnp.stack(got)
    return [lax.dynamic_index_in_dim(stacked, digit ^ g, 0, False) for g in range(radix)]


def sum_over_bits(value, axis, stages):
    for bits in stages:
        members = gather_bits(value, axis, bits)
        value = members[0]
        for other in members[1:]:
            value = value + other
    return value


def bit_stages(bits):
    return [bits[b : b + 2] for b in range(0, len(bits), 2)]


def group_sum(value, axis):
    count = lax.axis_size(axis).bit_length() - 1
    pairs = [(s, s ^ 1) for s in range(lax.axis_size(axis))]
    low = (lax.axis_index(axis) & 1) == 0
    half = value.shape[1] // 2
    first = value[:, :half]
    second = value[:, half:]
    arrived = lax.ppermute(jnp.where(low, second, first), axis, pairs)
    mine = jnp.where(low, first + arrived, arrived + second)
    mine = sum_over_bits(mine, axis, bit_stages(list(range(1, count))))
    other = lax.ppermute(mine, axis, pairs)
    return jnp.concatenate([jnp.where(low, mine, other), jnp.where(low, other, mine)], axis=1)


def pair_split_sum(value, axis, split_axis):
    count = lax.axis_size(axis).bit_length() - 1
    value = sum_over_bits(value, axis, [[0]])
    half = value.shape[split_axis] // 2
    low = (lax.axis_index(axis) & 1) == 0
    first = lax.slice_in_dim(value, 0, half, axis=split_axis)
    second = lax.slice_in_dim(value, half, 2 * half, axis=split_axis)
    mine = jnp.where(low, first, second)
    mine = sum_over_bits(mine, axis, bit_stages(list(range(1, count))))
    other = lax.ppermute(
        mine, axis, [(s, s ^ 1) for s in range(lax.axis_size(axis))]
    )
    return jnp.concatenate(
        [jnp.where(low, mine, other), jnp.where(low, other, mine)], axis=split_axis
    )


def scatter_groups(blocks, axis):
    size = lax.axis_size(axis)
    me = lax.axis_index(axis)
    for stride, radix in digit_groups(size):
        digit = (me // stride) % radix
        rest = blocks.shape[0] // radix
        split = blocks.reshape((rest, radix) + blocks.shape[1:])
        total = lax.dynamic_index_in_dim(split, digit, 1, False)
        for k in range(1, radix):
            pairs = [(s, s ^ (k * stride)) for s in range(size)]
            give = lax.dynamic_index_in_dim(split, digit ^ k, 1, False)
            total = total + lax.ppermute(give, axis, pairs)
        blocks = total
    return blocks[0]


def split_dot(spec, low, wide):
    high = wide.astype(BF16)
    rest = (wide - high.astype(F32)).astype(BF16)
    return jnp.einsum(spec, low, high, preferred_element_type=F32) + jnp.einsum(
        spec, low, rest, preferred_element_type=F32
    )


def combine_members(members, rows):
    def unpack(a):
        stats = a[:, rows:, :].reshape(a.shape[0], 4, rows)
        return a[:, :rows, :], stats[:, 0], stats[:, 1], stats[:, 2], stats[:, 3]

    parts = [unpack(a) for a in members]
    peak = parts[0][1]
    cpeak = parts[0][3]
    for p in parts[1:]:
        peak = jnp.maximum(peak, p[1])
        cpeak = jnp.maximum(cpeak, p[3])
    numer = denom = cdenom = None
    for p in parts:
        f = jnp.exp(p[1] - peak)
        g = jnp.exp(p[3] - cpeak)
        n_term = p[0] * f[..., None]
        numer = n_term if numer is None else numer + n_term
        denom = p[2] * f if denom is None else denom + p[2] * f
        cdenom = p[4] * g if cdenom is None else cdenom + p[4] * g
    return numer, peak, denom, cpeak, cdenom


def pack(numer, peak, denom, cpeak, cdenom):
    heads, rows, width = numer.shape
    stats = jnp.stack([peak, denom, cpeak, cdenom], axis=1).reshape(heads, 4 * rows // width, width)
    return jnp.concatenate([numer, stats], axis=1)


def per_device(queries, cache_keys, cache_values, selected):
    head_count, query_rows, head_width = queries.shape
    key_rows = cache_keys.shape[1]
    order_size = selected.shape[1]
    row_devices = lax.axis_size("pb")
    col_devices = lax.axis_size("kv")
    col_len = order_size // col_devices
    score_scale = head_width ** (-0.5)
    me_kv = lax.axis_index("kv")

    local_pos = me_kv * key_rows + jnp.arange(key_rows, dtype=jnp.int32)
    owned = selected[:, :, None] == local_pos[None, None, :]
    picked = jnp.einsum(
        "hak,hkd->had", owned.astype(BF16), cache_keys, preferred_element_type=F32
    ).astype(BF16)
    kept_mask = jnp.any(owned, axis=1)
    blocks = picked.reshape(head_count, col_devices, col_len, head_width).transpose(1, 0, 2, 3)
    chosen_block = scatter_groups(blocks, "kv")

    scores = (
        jnp.einsum("hqd,hkd->hqk", queries, cache_keys, preferred_element_type=F32) * score_scale
    )
    peak = jnp.max(scores, axis=-1)
    weights = jnp.exp(scores - peak[..., None])
    denom = jnp.sum(weights, axis=-1)
    w_high = weights.astype(BF16)
    w_low = (weights - w_high.astype(F32)).astype(BF16)
    numer = jnp.einsum(
        "hqk,hkd->hqd", w_high, cache_values, preferred_element_type=F32
    ) + jnp.einsum("hqk,hkd->hqd", w_low, cache_values, preferred_element_type=F32)
    floor = jnp.float32(-1e30)
    kept_scores = jnp.where(kept_mask[:, None, :], scores, floor)
    cpeak = jnp.max(kept_scores, axis=-1)
    cweights = jnp.where(kept_mask[:, None, :], jnp.exp(kept_scores - cpeak[..., None]), 0.0)
    cdenom = jnp.sum(cweights, axis=-1)

    stat_bits = (col_devices.bit_length() - 1) if isinstance(col_devices, int) else 4
    packed = pack(numer, peak, denom, cpeak, cdenom)
    members = gather_bits(packed, "kv", [0])
    numer, peak, denom, cpeak, cdenom = combine_members(members, query_rows)
    half = query_rows // 2
    low = (me_kv & 1) == 0
    halves = [
        pack(*(a[:, :half] for a in (numer, peak, denom, cpeak, cdenom))),
        pack(*(a[:, half:] for a in (numer, peak, denom, cpeak, cdenom))),
    ]
    packed = jnp.where(low, halves[0], halves[1])
    for bits in bit_stages(list(range(1, stat_bits))):
        members = gather_bits(packed, "kv", bits)
        packed = pack(*combine_members(members, half))
    other = lax.ppermute(packed, "kv", [(s, s ^ 1) for s in range(col_devices)])
    first_half = combine_members([jnp.where(low, packed, other)], half)
    second_half = combine_members([jnp.where(low, other, packed)], half)
    numer, peak, denom, cpeak, cdenom = (
        jnp.concatenate([a, b], axis=1) for a, b in zip(first_half, second_half)
    )
    attended = (numer / denom[..., None]).astype(BF16)

    compact = (
        jnp.einsum("hqd,hkd->hqk", queries, chosen_block, preferred_element_type=F32)
        * score_scale
    )
    probs = (jnp.exp(compact - cpeak[..., None]) / cdenom[..., None]).astype(BF16)

    weighting = order_size / (query_rows * row_devices)
    rhs_part = jnp.einsum("hqa,hqd->had", probs, attended, preferred_element_type=F32)
    rhs = group_sum(rhs_part, "pb") * weighting

    def gram_times(vec):
        across = pair_split_sum(split_dot("hqa,had->hqd", probs, vec), "kv", 1)
        back = group_sum(split_dot("hqa,hqd->had", probs, across), "pb")
        return back * weighting + ridge_weight * vec

    sigma = theta_mid / delta_half
    solution = jnp.zeros_like(rhs)
    resid = rhs
    direction = rhs / theta_mid
    recur_now = 1.0 / sigma
    for iteration in range(STEPS):
        solution = solution + direction
        resid = resid - gram_times(direction)
        recur_next = 1.0 / (2.0 * sigma - recur_now)
        direction = recur_next * recur_now * direction + 2.0 * recur_next / delta_half * resid
        recur_now = recur_next
    return (solution, resid)


def solution(mesh):
    in_specs = (P(None, "pb", None), P(None, "kv", None), P(None, "kv", None), P())
    out_specs = (P(None, "kv", None), P(None, "kv", None))
    return jax.shard_map(
        per_device, mesh=mesh, in_specs=in_specs, out_specs=out_specs, check_vma=False
    )
```

```python
import jax
import jax.numpy as jnp
from jax import lax
from jax.sharding import PartitionSpec as P

STEPS = 3


ridge_weight = 0.1
theta_mid = 1.1
delta_half = 1.0

F32 = jnp.float32
BF16 = jnp.bfloat16


def digit_groups(size):
    groups = []
    bit = 1
    while bit < size:
        radix = 4 if bit * 4 <= size else 2
        groups.append((bit, radix))
        bit *= radix
    return groups


def gather_group(value, axis, stride, radix):
    size = lax.axis_size(axis)
    me = lax.axis_index(axis)
    digit = (me // stride) % radix
    got = [value]
    for k in range(1, radix):
        pairs = [(s, s ^ (k * stride)) for s in range(size)]
        got.append(jax.tree.map(lambda a: lax.ppermute(a, axis, pairs), value))
    stacked = jax.tree.map(lambda *a: jnp.stack(a), *got)
    return [
        jax.tree.map(lambda a: lax.dynamic_index_in_dim(a, digit ^ g, 0, False), stacked)
        for g in range(radix)
    ]


def gather_bits(value, axis, bits):
    size = lax.axis_size(axis)
    me = lax.axis_index(axis)
    digit = sum(((me >> b) & 1) << t for t, b in enumerate(bits))
    radix = 1 << len(bits)
    got = [value]
    for k in range(1, radix):
        mask = sum(((k >> t) & 1) << b for t, b in enumerate(bits))
        pairs = [(s, s ^ mask) for s in range(size)]
        got.append(lax.ppermute(value, axis, pairs))
    stacked = jnp.stack(got)
    return [lax.dynamic_index_in_dim(stacked, digit ^ g, 0, False) for g in range(radix)]


def sum_over_bits(value, axis, stages):
    for bits in stages:
        members = gather_bits(value, axis, bits)
        value = members[0]
        for other in members[1:]:
            value = value + other
    return value


def bit_stages(bits):
    return [[b] for b in bits]


def group_sum(value, axis):
    count = lax.axis_size(axis).bit_length() - 1
    pairs = [(s, s ^ 1) for s in range(lax.axis_size(axis))]
    low = (lax.axis_index(axis) & 1) == 0
    half = value.shape[1] // 2
    first = value[:, :half]
    second = value[:, half:]
    arrived = lax.ppermute(jnp.where(low, second, first), axis, pairs)
    mine = jnp.where(low, first + arrived, arrived + second)
    mine = sum_over_bits(mine, axis, bit_stages(list(range(1, count))))
    other = lax.ppermute(mine, axis, pairs)
    return jnp.concatenate([jnp.where(low, mine, other), jnp.where(low, other, mine)], axis=1)


def pair_split_sum(value, axis, split_axis):
    count = lax.axis_size(axis).bit_length() - 1
    value = sum_over_bits(value, axis, [[0]])
    half = value.shape[split_axis] // 2
    low = (lax.axis_index(axis) & 1) == 0
    first = lax.slice_in_dim(value, 0, half, axis=split_axis)
    second = lax.slice_in_dim(value, half, 2 * half, axis=split_axis)
    mine = jnp.where(low, first, second)
    mine = sum_over_bits(mine, axis, bit_stages(list(range(1, count))))
    other = lax.ppermute(
        mine, axis, [(s, s ^ 1) for s in range(lax.axis_size(axis))]
    )
    return jnp.concatenate(
        [jnp.where(low, mine, other), jnp.where(low, other, mine)], axis=split_axis
    )


def scatter_groups(blocks, axis):
    size = lax.axis_size(axis)
    me = lax.axis_index(axis)
    for stride, radix in digit_groups(size):
        digit = (me // stride) % radix
        rest = blocks.shape[0] // radix
        split = blocks.reshape((rest, radix) + blocks.shape[1:])
        total = lax.dynamic_index_in_dim(split, digit, 1, False)
        for k in range(1, radix):
            pairs = [(s, s ^ (k * stride)) for s in range(size)]
            give = lax.dynamic_index_in_dim(split, digit ^ k, 1, False)
            total = total + lax.ppermute(give, axis, pairs)
        blocks = total
    return blocks[0]


def split_dot(spec, low, wide):
    high = wide.astype(BF16)
    rest = (wide - high.astype(F32)).astype(BF16)
    return jnp.einsum(spec, low, high, preferred_element_type=F32) + jnp.einsum(
        spec, low, rest, preferred_element_type=F32
    )


def combine_members(members, rows):
    def unpack(a):
        stats = a[:, rows:, :].reshape(a.shape[0], 4, rows)
        return a[:, :rows, :], stats[:, 0], stats[:, 1], stats[:, 2], stats[:, 3]

    parts = [unpack(a) for a in members]
    peak = parts[0][1]
    cpeak = parts[0][3]
    for p in parts[1:]:
        peak = jnp.maximum(peak, p[1])
        cpeak = jnp.maximum(cpeak, p[3])
    numer = denom = cdenom = None
    for p in parts:
        f = jnp.exp(p[1] - peak)
        g = jnp.exp(p[3] - cpeak)
        n_term = p[0] * f[..., None]
        numer = n_term if numer is None else numer + n_term
        denom = p[2] * f if denom is None else denom + p[2] * f
        cdenom = p[4] * g if cdenom is None else cdenom + p[4] * g
    return numer, peak, denom, cpeak, cdenom


def pack(numer, peak, denom, cpeak, cdenom):
    heads, rows, width = numer.shape
    stats = jnp.stack([peak, denom, cpeak, cdenom], axis=1).reshape(heads, 4 * rows // width, width)
    return jnp.concatenate([numer, stats], axis=1)


def per_device(queries, cache_keys, cache_values, selected):
    head_count, query_rows, head_width = queries.shape
    key_rows = cache_keys.shape[1]
    order_size = selected.shape[1]
    row_devices = lax.axis_size("pb")
    col_devices = lax.axis_size("kv")
    col_len = order_size // col_devices
    score_scale = head_width ** (-0.5)
    me_kv = lax.axis_index("kv")

    local_pos = me_kv * key_rows + jnp.arange(key_rows, dtype=jnp.int32)
    owned = selected[:, :, None] == local_pos[None, None, :]
    picked = jnp.einsum(
        "hak,hkd->had", owned.astype(BF16), cache_keys, preferred_element_type=F32
    ).astype(BF16)
    kept_mask = jnp.any(owned, axis=1)
    blocks = picked.reshape(head_count, col_devices, col_len, head_width).transpose(1, 0, 2, 3)
    chosen_block = scatter_groups(blocks, "kv")

    scores = (
        jnp.einsum("hqd,hkd->hqk", queries, cache_keys, preferred_element_type=F32) * score_scale
    )
    peak = jnp.max(scores, axis=-1)
    weights = jnp.exp(scores - peak[..., None])
    denom = jnp.sum(weights, axis=-1)
    w_high = weights.astype(BF16)
    w_low = (weights - w_high.astype(F32)).astype(BF16)
    numer = jnp.einsum(
        "hqk,hkd->hqd", w_high, cache_values, preferred_element_type=F32
    ) + jnp.einsum("hqk,hkd->hqd", w_low, cache_values, preferred_element_type=F32)
    floor = jnp.float32(-1e30)
    kept_scores = jnp.where(kept_mask[:, None, :], scores, floor)
    cpeak = jnp.max(kept_scores, axis=-1)
    cweights = jnp.where(kept_mask[:, None, :], jnp.exp(kept_scores - cpeak[..., None]), 0.0)
    cdenom = jnp.sum(cweights, axis=-1)

    stat_bits = (col_devices.bit_length() - 1) if isinstance(col_devices, int) else 4
    packed = pack(numer, peak, denom, cpeak, cdenom)
    members = gather_bits(packed, "kv", [0])
    numer, peak, denom, cpeak, cdenom = combine_members(members, query_rows)
    half = query_rows // 2
    low = (me_kv & 1) == 0
    halves = [
        pack(*(a[:, :half] for a in (numer, peak, denom, cpeak, cdenom))),
        pack(*(a[:, half:] for a in (numer, peak, denom, cpeak, cdenom))),
    ]
    packed = jnp.where(low, halves[0], halves[1])
    for bits in bit_stages(list(range(1, stat_bits))):
        members = gather_bits(packed, "kv", bits)
        packed = pack(*combine_members(members, half))
    other = lax.ppermute(packed, "kv", [(s, s ^ 1) for s in range(col_devices)])
    first_half = combine_members([jnp.where(low, packed, other)], half)
    second_half = combine_members([jnp.where(low, other, packed)], half)
    numer, peak, denom, cpeak, cdenom = (
        jnp.concatenate([a, b], axis=1) for a, b in zip(first_half, second_half)
    )
    attended = (numer / denom[..., None]).astype(BF16)

    compact = (
        jnp.einsum("hqd,hkd->hqk", queries, chosen_block, preferred_element_type=F32)
        * score_scale
    )
    probs = (jnp.exp(compact - cpeak[..., None]) / cdenom[..., None]).astype(BF16)

    weighting = order_size / (query_rows * row_devices)
    rhs_part = jnp.einsum("hqa,hqd->had", probs, attended, preferred_element_type=F32)
    rhs = group_sum(rhs_part, "pb") * weighting

    def gram_times(vec):
        across = pair_split_sum(split_dot("hqa,had->hqd", probs, vec), "kv", 1)
        back = group_sum(split_dot("hqa,hqd->had", probs, across), "pb")
        return back * weighting + ridge_weight * vec

    sigma = theta_mid / delta_half
    solution = jnp.zeros_like(rhs)
    resid = rhs
    direction = rhs / theta_mid
    recur_now = 1.0 / sigma
    for iteration in range(STEPS):
        solution = solution + direction
        resid = resid - gram_times(direction)
        recur_next = 1.0 / (2.0 * sigma - recur_now)
        direction = recur_next * recur_now * direction + 2.0 * recur_next / delta_half * resid
        recur_now = recur_next
    return (solution, resid)


def solution(mesh):
    in_specs = (P(None, "pb", None), P(None, "kv", None), P(None, "kv", None), P())
    out_specs = (P(None, "kv", None), P(None, "kv", None))
    return jax.shard_map(
        per_device, mesh=mesh, in_specs=in_specs, out_specs=out_specs, check_vma=False
    )
```

```python
import jax
import jax.numpy as jnp
from jax import lax
from jax.sharding import PartitionSpec as P

STEPS = 3


ridge_weight = 0.1
theta_mid = 1.1
delta_half = 1.0

F32 = jnp.float32
BF16 = jnp.bfloat16


def digit_groups(size):
    groups = []
    bit = 1
    while bit < size:
        radix = 4 if bit * 4 <= size else 2
        groups.append((bit, radix))
        bit *= radix
    return groups


def gather_group(value, axis, stride, radix):
    size = lax.axis_size(axis)
    me = lax.axis_index(axis)
    digit = (me // stride) % radix
    got = [value]
    for k in range(1, radix):
        pairs = [(s, s ^ (k * stride)) for s in range(size)]
        got.append(jax.tree.map(lambda a: lax.ppermute(a, axis, pairs), value))
    stacked = jax.tree.map(lambda *a: jnp.stack(a), *got)
    return [
        jax.tree.map(lambda a: lax.dynamic_index_in_dim(a, digit ^ g, 0, False), stacked)
        for g in range(radix)
    ]


def gather_bits(value, axis, bits):
    size = lax.axis_size(axis)
    me = lax.axis_index(axis)
    digit = sum(((me >> b) & 1) << t for t, b in enumerate(bits))
    radix = 1 << len(bits)
    got = [value]
    for k in range(1, radix):
        mask = sum(((k >> t) & 1) << b for t, b in enumerate(bits))
        pairs = [(s, s ^ mask) for s in range(size)]
        got.append(lax.ppermute(value, axis, pairs))
    stacked = jnp.stack(got)
    return [lax.dynamic_index_in_dim(stacked, digit ^ g, 0, False) for g in range(radix)]


def sum_over_bits(value, axis, stages):
    for bits in stages:
        members = gather_bits(value, axis, bits)
        value = members[0]
        for other in members[1:]:
            value = value + other
    return value


def bit_stages(bits):
    return [[b] for b in bits]


def group_sum(value, axis):
    count = lax.axis_size(axis).bit_length() - 1
    pairs = [(s, s ^ 1) for s in range(lax.axis_size(axis))]
    low = (lax.axis_index(axis) & 1) == 0
    half = value.shape[1] // 2
    first = value[:, :half]
    second = value[:, half:]
    arrived = lax.ppermute(jnp.where(low, second, first), axis, pairs)
    mine = jnp.where(low, first + arrived, arrived + second)
    mine = sum_over_bits(mine, axis, bit_stages(list(range(1, count))))
    other = lax.ppermute(mine, axis, pairs)
    return jnp.concatenate([jnp.where(low, mine, other), jnp.where(low, other, mine)], axis=1)


def pair_split_sum(value, axis, split_axis):
    count = lax.axis_size(axis).bit_length() - 1
    value = sum_over_bits(value, axis, [[0]])
    half = value.shape[split_axis] // 2
    low = (lax.axis_index(axis) & 1) == 0
    first = lax.slice_in_dim(value, 0, half, axis=split_axis)
    second = lax.slice_in_dim(value, half, 2 * half, axis=split_axis)
    mine = jnp.where(low, first, second)
    mine = sum_over_bits(mine, axis, bit_stages(list(range(1, count))))
    other = lax.ppermute(
        mine, axis, [(s, s ^ 1) for s in range(lax.axis_size(axis))]
    )
    return jnp.concatenate(
        [jnp.where(low, mine, other), jnp.where(low, other, mine)], axis=split_axis
    )


def scatter_groups(blocks, axis):
    size = lax.axis_size(axis)
    me = lax.axis_index(axis)
    for stride, radix in digit_groups(size):
        digit = (me // stride) % radix
        rest = blocks.shape[0] // radix
        split = blocks.reshape((rest, radix) + blocks.shape[1:])
        total = lax.dynamic_index_in_dim(split, digit, 1, False)
        for k in range(1, radix):
            pairs = [(s, s ^ (k * stride)) for s in range(size)]
            give = lax.dynamic_index_in_dim(split, digit ^ k, 1, False)
            total = total + lax.ppermute(give, axis, pairs)
        blocks = total
    return blocks[0]


def split_dot(spec, low, wide):
    high = wide.astype(BF16)
    rest = (wide - high.astype(F32)).astype(BF16)
    return jnp.einsum(spec, low, high, preferred_element_type=F32) + jnp.einsum(
        spec, low, rest, preferred_element_type=F32
    )


def combine_members(members, rows):
    def unpack(a):
        stats = a[:, rows:, :].reshape(a.shape[0], 4, rows)
        return a[:, :rows, :], stats[:, 0], stats[:, 1], stats[:, 2], stats[:, 3]

    parts = [unpack(a) for a in members]
    peak = parts[0][1]
    cpeak = parts[0][3]
    for p in parts[1:]:
        peak = jnp.maximum(peak, p[1])
        cpeak = jnp.maximum(cpeak, p[3])
    numer = denom = cdenom = None
    for p in parts:
        f = jnp.exp(p[1] - peak)
        g = jnp.exp(p[3] - cpeak)
        n_term = p[0] * f[..., None]
        numer = n_term if numer is None else numer + n_term
        denom = p[2] * f if denom is None else denom + p[2] * f
        cdenom = p[4] * g if cdenom is None else cdenom + p[4] * g
    return numer, peak, denom, cpeak, cdenom


def pack(numer, peak, denom, cpeak, cdenom):
    heads, rows, width = numer.shape
    stats = jnp.stack([peak, denom, cpeak, cdenom], axis=1).reshape(heads, 4 * rows // width, width)
    return jnp.concatenate([numer, stats], axis=1)


def per_device(queries, cache_keys, cache_values, selected):
    head_count, query_rows, head_width = queries.shape
    key_rows = cache_keys.shape[1]
    order_size = selected.shape[1]
    row_devices = lax.axis_size("pb")
    col_devices = lax.axis_size("kv")
    col_len = order_size // col_devices
    score_scale = head_width ** (-0.5)
    me_kv = lax.axis_index("kv")

    local_pos = me_kv * key_rows + jnp.arange(key_rows, dtype=jnp.int32)
    owned = selected[:, :, None] == local_pos[None, None, :]
    picked = jnp.einsum(
        "hak,hkd->had", owned.astype(BF16), cache_keys, preferred_element_type=F32
    ).astype(BF16)
    kept_mask = jnp.any(owned, axis=1)
    blocks = picked.reshape(head_count, col_devices, col_len, head_width).transpose(1, 0, 2, 3)
    chosen_block = scatter_groups(blocks, "kv")

    scores = (
        jnp.einsum("hqd,hkd->hqk", queries, cache_keys, preferred_element_type=F32) * score_scale
    )
    peak = jnp.max(scores, axis=-1)
    weights = jnp.exp(scores - peak[..., None])
    denom = jnp.sum(weights, axis=-1)
    w_high = weights.astype(BF16)
    w_low = (weights - w_high.astype(F32)).astype(BF16)
    numer = jnp.einsum(
        "hqk,hkd->hqd", w_high, cache_values, preferred_element_type=F32
    ) + jnp.einsum("hqk,hkd->hqd", w_low, cache_values, preferred_element_type=F32)
    floor = jnp.float32(-1e30)
    kept_scores = jnp.where(kept_mask[:, None, :], scores, floor)
    cpeak = jnp.max(kept_scores, axis=-1)
    cweights = jnp.where(kept_mask[:, None, :], jnp.exp(kept_scores - cpeak[..., None]), 0.0)
    cdenom = jnp.sum(cweights, axis=-1)

    stat_bits = (col_devices.bit_length() - 1) if isinstance(col_devices, int) else 4
    half = query_rows // 2
    low = (me_kv & 1) == 0
    halves = [
        pack(*(a[:, :half] for a in (numer, peak, denom, cpeak, cdenom))),
        pack(*(a[:, half:] for a in (numer, peak, denom, cpeak, cdenom))),
    ]
    keep = jnp.where(low, halves[0], halves[1])
    arrived = lax.ppermute(
        jnp.where(low, halves[1], halves[0]), "kv", [(s, s ^ 1) for s in range(col_devices)]
    )
    packed = pack(
        *combine_members([jnp.where(low, keep, arrived), jnp.where(low, arrived, keep)], half)
    )
    for bits in bit_stages(list(range(1, stat_bits))):
        members = gather_bits(packed, "kv", bits)
        packed = pack(*combine_members(members, half))
    other = lax.ppermute(packed, "kv", [(s, s ^ 1) for s in range(col_devices)])
    first_half = combine_members([jnp.where(low, packed, other)], half)
    second_half = combine_members([jnp.where(low, other, packed)], half)
    numer, peak, denom, cpeak, cdenom = (
        jnp.concatenate([a, b], axis=1) for a, b in zip(first_half, second_half)
    )
    attended = (numer / denom[..., None]).astype(BF16)

    compact = (
        jnp.einsum("hqd,hkd->hqk", queries, chosen_block, preferred_element_type=F32)
        * score_scale
    )
    probs = (jnp.exp(compact - cpeak[..., None]) / cdenom[..., None]).astype(BF16)

    weighting = order_size / (query_rows * row_devices)
    rhs_part = jnp.einsum("hqa,hqd->had", probs, attended, preferred_element_type=F32)
    rhs = group_sum(rhs_part, "pb") * weighting

    def gram_times(vec):
        across = group_sum(split_dot("hqa,had->hqd", probs, vec), "kv")
        back = group_sum(split_dot("hqa,hqd->had", probs, across), "pb")
        return back * weighting + ridge_weight * vec

    sigma = theta_mid / delta_half
    solution = jnp.zeros_like(rhs)
    resid = rhs
    direction = rhs / theta_mid
    recur_now = 1.0 / sigma
    for iteration in range(STEPS):
        solution = solution + direction
        resid = resid - gram_times(direction)
        recur_next = 1.0 / (2.0 * sigma - recur_now)
        direction = recur_next * recur_now * direction + 2.0 * recur_next / delta_half * resid
        recur_now = recur_next
    return (solution, resid)


def solution(mesh):
    in_specs = (P(None, "pb", None), P(None, "kv", None), P(None, "kv", None), P())
    out_specs = (P(None, "kv", None), P(None, "kv", None))
    return jax.shard_map(
        per_device, mesh=mesh, in_specs=in_specs, out_specs=out_specs, check_vma=False
    )
```

```python
import jax
import jax.numpy as jnp
from jax import lax
from jax.sharding import PartitionSpec as P

STEPS = 3


ridge_weight = 0.1
theta_mid = 1.1
delta_half = 1.0

F32 = jnp.float32
BF16 = jnp.bfloat16


def digit_groups(size):
    groups = []
    bit = 1
    while bit < size:
        radix = 4 if bit * 4 <= size else 2
        groups.append((bit, radix))
        bit *= radix
    return groups


def gather_group(value, axis, stride, radix):
    size = lax.axis_size(axis)
    me = lax.axis_index(axis)
    digit = (me // stride) % radix
    got = [value]
    for k in range(1, radix):
        pairs = [(s, s ^ (k * stride)) for s in range(size)]
        got.append(jax.tree.map(lambda a: lax.ppermute(a, axis, pairs), value))
    stacked = jax.tree.map(lambda *a: jnp.stack(a), *got)
    return [
        jax.tree.map(lambda a: lax.dynamic_index_in_dim(a, digit ^ g, 0, False), stacked)
        for g in range(radix)
    ]


def gather_bits(value, axis, bits):
    size = lax.axis_size(axis)
    me = lax.axis_index(axis)
    digit = sum(((me >> b) & 1) << t for t, b in enumerate(bits))
    radix = 1 << len(bits)
    got = [value]
    for k in range(1, radix):
        mask = sum(((k >> t) & 1) << b for t, b in enumerate(bits))
        pairs = [(s, s ^ mask) for s in range(size)]
        got.append(lax.ppermute(value, axis, pairs))
    stacked = jnp.stack(got)
    return [lax.dynamic_index_in_dim(stacked, digit ^ g, 0, False) for g in range(radix)]


def sum_over_bits(value, axis, stages):
    for bits in stages:
        members = gather_bits(value, axis, bits)
        value = members[0]
        for other in members[1:]:
            value = value + other
    return value


def bit_stages(bits):
    return [[b] for b in bits]


def group_sum(value, axis):
    count = lax.axis_size(axis).bit_length() - 1
    pairs = [(s, s ^ 1) for s in range(lax.axis_size(axis))]
    low = (lax.axis_index(axis) & 1) == 0
    half = value.shape[1] // 2
    first = value[:, :half]
    second = value[:, half:]
    arrived = lax.ppermute(jnp.where(low, second, first), axis, pairs)
    mine = jnp.where(low, first + arrived, arrived + second)
    mine = sum_over_bits(mine, axis, bit_stages(list(range(1, count))))
    other = lax.ppermute(mine, axis, pairs)
    return jnp.concatenate([jnp.where(low, mine, other), jnp.where(low, other, mine)], axis=1)


def pair_split_sum(value, axis, split_axis):
    count = lax.axis_size(axis).bit_length() - 1
    value = sum_over_bits(value, axis, [[0]])
    half = value.shape[split_axis] // 2
    low = (lax.axis_index(axis) & 1) == 0
    first = lax.slice_in_dim(value, 0, half, axis=split_axis)
    second = lax.slice_in_dim(value, half, 2 * half, axis=split_axis)
    mine = jnp.where(low, first, second)
    mine = sum_over_bits(mine, axis, bit_stages(list(range(1, count))))
    other = lax.ppermute(
        mine, axis, [(s, s ^ 1) for s in range(lax.axis_size(axis))]
    )
    return jnp.concatenate(
        [jnp.where(low, mine, other), jnp.where(low, other, mine)], axis=split_axis
    )


def scatter_groups(blocks, axis, hold):
    size = lax.axis_size(axis)
    me = lax.axis_index(axis)
    for level, (stride, radix) in enumerate(digit_groups(size)):
        if level == 1:
            blocks, hold = lax.optimization_barrier((blocks, hold))
        digit = (me // stride) % radix
        rest = blocks.shape[0] // radix
        split = blocks.reshape((rest, radix) + blocks.shape[1:])
        total = lax.dynamic_index_in_dim(split, digit, 1, False)
        for k in range(1, radix):
            pairs = [(s, s ^ (k * stride)) for s in range(size)]
            give = lax.dynamic_index_in_dim(split, digit ^ k, 1, False)
            total = total + lax.ppermute(give, axis, pairs)
        blocks = total
    return blocks[0], hold


def split_dot(spec, low, wide):
    high = wide.astype(BF16)
    rest = (wide - high.astype(F32)).astype(BF16)
    return jnp.einsum(spec, low, high, preferred_element_type=F32) + jnp.einsum(
        spec, low, rest, preferred_element_type=F32
    )


def combine_members(members, rows):
    def unpack(a):
        stats = a[:, rows:, :].reshape(a.shape[0], 4, rows)
        return a[:, :rows, :], stats[:, 0], stats[:, 1], stats[:, 2], stats[:, 3]

    parts = [unpack(a) for a in members]
    peak = parts[0][1]
    cpeak = parts[0][3]
    for p in parts[1:]:
        peak = jnp.maximum(peak, p[1])
        cpeak = jnp.maximum(cpeak, p[3])
    numer = denom = cdenom = None
    for p in parts:
        f = jnp.exp(p[1] - peak)
        g = jnp.exp(p[3] - cpeak)
        n_term = p[0] * f[..., None]
        numer = n_term if numer is None else numer + n_term
        denom = p[2] * f if denom is None else denom + p[2] * f
        cdenom = p[4] * g if cdenom is None else cdenom + p[4] * g
    return numer, peak, denom, cpeak, cdenom


def pack(numer, peak, denom, cpeak, cdenom):
    heads, rows, width = numer.shape
    stats = jnp.stack([peak, denom, cpeak, cdenom], axis=1).reshape(heads, 4 * rows // width, width)
    return jnp.concatenate([numer, stats], axis=1)


def per_device(queries, cache_keys, cache_values, selected):
    head_count, query_rows, head_width = queries.shape
    key_rows = cache_keys.shape[1]
    order_size = selected.shape[1]
    row_devices = lax.axis_size("pb")
    col_devices = lax.axis_size("kv")
    col_len = order_size // col_devices
    score_scale = head_width ** (-0.5)
    me_kv = lax.axis_index("kv")

    local_pos = me_kv * key_rows + jnp.arange(key_rows, dtype=jnp.int32)
    owned = selected[:, :, None] == local_pos[None, None, :]
    picked = jnp.einsum(
        "hak,hkd->had", owned.astype(BF16), cache_keys, preferred_element_type=F32
    ).astype(BF16)
    kept_mask = jnp.any(owned, axis=1)
    blocks = picked.reshape(head_count, col_devices, col_len, head_width).transpose(1, 0, 2, 3)
    chosen_block, queries = scatter_groups(blocks, "kv", queries)

    scores = (
        jnp.einsum("hqd,hkd->hqk", queries, cache_keys, preferred_element_type=F32) * score_scale
    )
    peak = jnp.max(scores, axis=-1)
    weights = jnp.exp(scores - peak[..., None])
    denom = jnp.sum(weights, axis=-1)
    w_high = weights.astype(BF16)
    w_low = (weights - w_high.astype(F32)).astype(BF16)
    numer = jnp.einsum(
        "hqk,hkd->hqd", w_high, cache_values, preferred_element_type=F32
    ) + jnp.einsum("hqk,hkd->hqd", w_low, cache_values, preferred_element_type=F32)
    floor = jnp.float32(-1e30)
    kept_scores = jnp.where(kept_mask[:, None, :], scores, floor)
    cpeak = jnp.max(kept_scores, axis=-1)
    cweights = jnp.where(kept_mask[:, None, :], jnp.exp(kept_scores - cpeak[..., None]), 0.0)
    cdenom = jnp.sum(cweights, axis=-1)

    stat_bits = (col_devices.bit_length() - 1) if isinstance(col_devices, int) else 4
    half = query_rows // 2
    low = (me_kv & 1) == 0
    halves = [
        pack(*(a[:, :half] for a in (numer, peak, denom, cpeak, cdenom))),
        pack(*(a[:, half:] for a in (numer, peak, denom, cpeak, cdenom))),
    ]
    keep = jnp.where(low, halves[0], halves[1])
    arrived = lax.ppermute(
        jnp.where(low, halves[1], halves[0]), "kv", [(s, s ^ 1) for s in range(col_devices)]
    )
    packed = pack(
        *combine_members([jnp.where(low, keep, arrived), jnp.where(low, arrived, keep)], half)
    )
    for bits in bit_stages(list(range(1, stat_bits))):
        members = gather_bits(packed, "kv", bits)
        packed = pack(*combine_members(members, half))
    other = lax.ppermute(packed, "kv", [(s, s ^ 1) for s in range(col_devices)])
    first_half = combine_members([jnp.where(low, packed, other)], half)
    second_half = combine_members([jnp.where(low, other, packed)], half)
    numer, peak, denom, cpeak, cdenom = (
        jnp.concatenate([a, b], axis=1) for a, b in zip(first_half, second_half)
    )
    attended = (numer / denom[..., None]).astype(BF16)

    compact = (
        jnp.einsum("hqd,hkd->hqk", queries, chosen_block, preferred_element_type=F32)
        * score_scale
    )
    probs = (jnp.exp(compact - cpeak[..., None]) / cdenom[..., None]).astype(BF16)

    weighting = order_size / (query_rows * row_devices)
    rhs_part = jnp.einsum("hqa,hqd->had", probs, attended, preferred_element_type=F32)
    rhs = group_sum(rhs_part, "pb") * weighting

    def gram_times(vec):
        across = group_sum(split_dot("hqa,had->hqd", probs, vec), "kv")
        back = group_sum(split_dot("hqa,hqd->had", probs, across), "pb")
        return back * weighting + ridge_weight * vec

    sigma = theta_mid / delta_half
    solution = jnp.zeros_like(rhs)
    resid = rhs
    direction = rhs / theta_mid
    recur_now = 1.0 / sigma
    for iteration in range(STEPS):
        solution = solution + direction
        resid = resid - gram_times(direction)
        recur_next = 1.0 / (2.0 * sigma - recur_now)
        direction = recur_next * recur_now * direction + 2.0 * recur_next / delta_half * resid
        recur_now = recur_next
    return (solution, resid)


def solution(mesh):
    in_specs = (P(None, "pb", None), P(None, "kv", None), P(None, "kv", None), P())
    out_specs = (P(None, "kv", None), P(None, "kv", None))
    return jax.shard_map(
        per_device, mesh=mesh, in_specs=in_specs, out_specs=out_specs, check_vma=False
    )
```

```python
import jax
import jax.numpy as jnp
from jax import lax
from jax.sharding import PartitionSpec as P

STEPS = 3


ridge_weight = 0.1
theta_mid = 1.1
delta_half = 1.0

F32 = jnp.float32
BF16 = jnp.bfloat16


def digit_groups(size):
    groups = []
    bit = 1
    while bit < size:
        radix = 4 if bit * 4 <= size else 2
        groups.append((bit, radix))
        bit *= radix
    return groups


def gather_group(value, axis, stride, radix):
    size = lax.axis_size(axis)
    me = lax.axis_index(axis)
    digit = (me // stride) % radix
    got = [value]
    for k in range(1, radix):
        pairs = [(s, s ^ (k * stride)) for s in range(size)]
        got.append(jax.tree.map(lambda a: lax.ppermute(a, axis, pairs), value))
    stacked = jax.tree.map(lambda *a: jnp.stack(a), *got)
    return [
        jax.tree.map(lambda a: lax.dynamic_index_in_dim(a, digit ^ g, 0, False), stacked)
        for g in range(radix)
    ]


def gather_bits(value, axis, bits):
    size = lax.axis_size(axis)
    me = lax.axis_index(axis)
    digit = sum(((me >> b) & 1) << t for t, b in enumerate(bits))
    radix = 1 << len(bits)
    got = [value]
    for k in range(1, radix):
        mask = sum(((k >> t) & 1) << b for t, b in enumerate(bits))
        pairs = [(s, s ^ mask) for s in range(size)]
        got.append(lax.ppermute(value, axis, pairs))
    stacked = jnp.stack(got)
    return [lax.dynamic_index_in_dim(stacked, digit ^ g, 0, False) for g in range(radix)]


def sum_over_bits(value, axis, stages):
    for bits in stages:
        members = gather_bits(value, axis, bits)
        value = members[0]
        for other in members[1:]:
            value = value + other
    return value


def bit_stages(bits):
    return [[b] for b in bits]


def group_sum(value, axis):
    count = lax.axis_size(axis).bit_length() - 1
    me = lax.axis_index(axis)
    depth = 2
    for bit in range(depth):
        pairs = [(s, s ^ (1 << bit)) for s in range(lax.axis_size(axis))]
        low = ((me >> bit) & 1) == 0
        half = value.shape[1] // 2
        first = value[:, :half]
        second = value[:, half:]
        arrived = lax.ppermute(jnp.where(low, second, first), axis, pairs)
        value = jnp.where(low, first + arrived, arrived + second)
    value = sum_over_bits(value, axis, bit_stages(list(range(depth, count))))
    for bit in reversed(range(depth)):
        pairs = [(s, s ^ (1 << bit)) for s in range(lax.axis_size(axis))]
        low = ((me >> bit) & 1) == 0
        other = lax.ppermute(value, axis, pairs)
        value = jnp.concatenate(
            [jnp.where(low, value, other), jnp.where(low, other, value)], axis=1
        )
    return value


def pair_split_sum(value, axis, split_axis):
    count = lax.axis_size(axis).bit_length() - 1
    value = sum_over_bits(value, axis, [[0]])
    half = value.shape[split_axis] // 2
    low = (lax.axis_index(axis) & 1) == 0
    first = lax.slice_in_dim(value, 0, half, axis=split_axis)
    second = lax.slice_in_dim(value, half, 2 * half, axis=split_axis)
    mine = jnp.where(low, first, second)
    mine = sum_over_bits(mine, axis, bit_stages(list(range(1, count))))
    other = lax.ppermute(
        mine, axis, [(s, s ^ 1) for s in range(lax.axis_size(axis))]
    )
    return jnp.concatenate(
        [jnp.where(low, mine, other), jnp.where(low, other, mine)], axis=split_axis
    )


def scatter_groups(blocks, axis):
    size = lax.axis_size(axis)
    me = lax.axis_index(axis)
    for stride, radix in digit_groups(size):
        digit = (me // stride) % radix
        rest = blocks.shape[0] // radix
        split = blocks.reshape((rest, radix) + blocks.shape[1:])
        total = lax.dynamic_index_in_dim(split, digit, 1, False)
        for k in range(1, radix):
            pairs = [(s, s ^ (k * stride)) for s in range(size)]
            give = lax.dynamic_index_in_dim(split, digit ^ k, 1, False)
            total = total + lax.ppermute(give, axis, pairs)
        blocks = total
    return blocks[0]


def split_dot(spec, low, wide):
    high = wide.astype(BF16)
    rest = (wide - high.astype(F32)).astype(BF16)
    return jnp.einsum(spec, low, high, preferred_element_type=F32) + jnp.einsum(
        spec, low, rest, preferred_element_type=F32
    )


def combine_members(members, rows):
    def unpack(a):
        stats = a[:, rows:, :].reshape(a.shape[0], 4, rows)
        return a[:, :rows, :], stats[:, 0], stats[:, 1], stats[:, 2], stats[:, 3]

    parts = [unpack(a) for a in members]
    peak = parts[0][1]
    cpeak = parts[0][3]
    for p in parts[1:]:
        peak = jnp.maximum(peak, p[1])
        cpeak = jnp.maximum(cpeak, p[3])
    numer = denom = cdenom = None
    for p in parts:
        f = jnp.exp(p[1] - peak)
        g = jnp.exp(p[3] - cpeak)
        n_term = p[0] * f[..., None]
        numer = n_term if numer is None else numer + n_term
        denom = p[2] * f if denom is None else denom + p[2] * f
        cdenom = p[4] * g if cdenom is None else cdenom + p[4] * g
    return numer, peak, denom, cpeak, cdenom


def pack(numer, peak, denom, cpeak, cdenom):
    heads, rows, width = numer.shape
    stats = jnp.stack([peak, denom, cpeak, cdenom], axis=1).reshape(heads, 4 * rows // width, width)
    return jnp.concatenate([numer, stats], axis=1)


def per_device(queries, cache_keys, cache_values, selected):
    head_count, query_rows, head_width = queries.shape
    key_rows = cache_keys.shape[1]
    order_size = selected.shape[1]
    row_devices = lax.axis_size("pb")
    col_devices = lax.axis_size("kv")
    col_len = order_size // col_devices
    score_scale = head_width ** (-0.5)
    me_kv = lax.axis_index("kv")

    local_pos = me_kv * key_rows + jnp.arange(key_rows, dtype=jnp.int32)
    owned = selected[:, :, None] == local_pos[None, None, :]
    picked = jnp.einsum(
        "hak,hkd->had", owned.astype(BF16), cache_keys, preferred_element_type=F32
    ).astype(BF16)
    kept_mask = jnp.any(owned, axis=1)
    blocks = picked.reshape(head_count, col_devices, col_len, head_width).transpose(1, 0, 2, 3)
    chosen_block = scatter_groups(blocks, "kv")

    scores = (
        jnp.einsum("hqd,hkd->hqk", queries, cache_keys, preferred_element_type=F32) * score_scale
    )
    peak = jnp.max(scores, axis=-1)
    weights = jnp.exp(scores - peak[..., None])
    denom = jnp.sum(weights, axis=-1)
    w_high = weights.astype(BF16)
    w_low = (weights - w_high.astype(F32)).astype(BF16)
    numer = jnp.einsum(
        "hqk,hkd->hqd", w_high, cache_values, preferred_element_type=F32
    ) + jnp.einsum("hqk,hkd->hqd", w_low, cache_values, preferred_element_type=F32)
    floor = jnp.float32(-1e30)
    kept_scores = jnp.where(kept_mask[:, None, :], scores, floor)
    cpeak = jnp.max(kept_scores, axis=-1)
    cweights = jnp.where(kept_mask[:, None, :], jnp.exp(kept_scores - cpeak[..., None]), 0.0)
    cdenom = jnp.sum(cweights, axis=-1)

    stat_bits = (col_devices.bit_length() - 1) if isinstance(col_devices, int) else 4
    half = query_rows // 2
    low = (me_kv & 1) == 0
    halves = [
        pack(*(a[:, :half] for a in (numer, peak, denom, cpeak, cdenom))),
        pack(*(a[:, half:] for a in (numer, peak, denom, cpeak, cdenom))),
    ]
    keep = jnp.where(low, halves[0], halves[1])
    arrived = lax.ppermute(
        jnp.where(low, halves[1], halves[0]), "kv", [(s, s ^ 1) for s in range(col_devices)]
    )
    packed = pack(
        *combine_members([jnp.where(low, keep, arrived), jnp.where(low, arrived, keep)], half)
    )
    for bits in bit_stages(list(range(1, stat_bits))):
        members = gather_bits(packed, "kv", bits)
        packed = pack(*combine_members(members, half))
    other = lax.ppermute(packed, "kv", [(s, s ^ 1) for s in range(col_devices)])
    first_half = combine_members([jnp.where(low, packed, other)], half)
    second_half = combine_members([jnp.where(low, other, packed)], half)
    numer, peak, denom, cpeak, cdenom = (
        jnp.concatenate([a, b], axis=1) for a, b in zip(first_half, second_half)
    )
    attended = (numer / denom[..., None]).astype(BF16)

    compact = (
        jnp.einsum("hqd,hkd->hqk", queries, chosen_block, preferred_element_type=F32)
        * score_scale
    )
    probs = (jnp.exp(compact - cpeak[..., None]) / cdenom[..., None]).astype(BF16)

    weighting = order_size / (query_rows * row_devices)
    rhs_part = jnp.einsum("hqa,hqd->had", probs, attended, preferred_element_type=F32)
    rhs = group_sum(rhs_part, "pb") * weighting

    def gram_times(vec):
        across = group_sum(split_dot("hqa,had->hqd", probs, vec), "kv")
        back = group_sum(split_dot("hqa,hqd->had", probs, across), "pb")
        return back * weighting + ridge_weight * vec

    sigma = theta_mid / delta_half
    solution = jnp.zeros_like(rhs)
    resid = rhs
    direction = rhs / theta_mid
    recur_now = 1.0 / sigma
    for iteration in range(STEPS):
        solution = solution + direction
        resid = resid - gram_times(direction)
        recur_next = 1.0 / (2.0 * sigma - recur_now)
        direction = recur_next * recur_now * direction + 2.0 * recur_next / delta_half * resid
        recur_now = recur_next
    return (solution, resid)


def solution(mesh):
    in_specs = (P(None, "pb", None), P(None, "kv", None), P(None, "kv", None), P())
    out_specs = (P(None, "kv", None), P(None, "kv", None))
    return jax.shard_map(
        per_device, mesh=mesh, in_specs=in_specs, out_specs=out_specs, check_vma=False
    )
```
